1024 devices in a mesh: rep: 128 (over z, y_hi, core), fsdp: 8 (over x, y_lo).
Axes of the slice: x: 4, y: 4 (y_hi: 2, y_lo: 2; y = y_hi * 2 + y_lo), z: 32, core: 2. Of those that a mesh axis runs over, the one named last changes fastest.
Arguments:
- tokens: bfloat16 [128, 512, 5120], P('rep'), may hold values from -6 to 6
- cotangent: bfloat16 [128, 512, 13824], P('rep', None, 'fsdp'), may hold values from -0.119628906 to 0.119628906
- adapter_a: float32 [128, 32, 5120], P('rep', None, 'fsdp'), may hold values from -6 to 6
- adapter_b: float32 [128, 32, 13824], P('rep', None, 'fsdp'), may hold values from -6 to 6
- moment_a: float32 [128, 32, 5120], P('rep', None, 'fsdp'), may hold values from -3 to 3
- moment_b: float32 [128, 32, 13824], P('rep', None, 'fsdp'), may hold values from -3 to 3
- step_start: int32 [1], replicated, may hold values from 0 to 63
Outputs:
- final_a: float32 [128, 32, 5120], P('rep', None, 'fsdp')
- final_b: float32 [128, 32, 13824], P('rep', None, 'fsdp')
The draws below stay inside these ranges and needn't reach their ends.
All inputs are finite; a program needn't handle non-finite values.
Results may differ from the reference program's by a relative error of at most 0.009.
Values may be sent and summed in bfloat16 or wider, within the bound.
No kernel may reach another device: no remote copies, remote signals or barrier semaphores. Data moves between devices by JAX's collectives and lax.ppermute only.
A program may use at most 32 MiB of HBM per device.

```python
import jax
import jax.numpy as jnp
from jax import lax

D = 5120
FF = 13824
R = 32
TOK_R = 512
STEPS = 3
REPLICAS = 128
N_REP = 128


def block_scale(key, shape, split, low, top_value):
    factor_of, own = 1.0, jax.random.fold_in(key, 6)
    for position, parts in split:
        heights = jnp.exp(jax.random.uniform(jax.random.fold_in(own, position), (parts,), jnp.float32, low / len(split), top_value / len(split)))
        factor_of = factor_of * jnp.repeat(heights, shape[position] // parts).reshape([-1 if axis == position else 1 for axis in range(len(shape))])
    return factor_of


def gaussian(stream_key, dims, scale, limit, cuts=(), dtype=jnp.bfloat16):
    result = scale * jax.random.normal(stream_key, dims, jnp.float32)
    if cuts:
        result = result * block_scale(stream_key, dims, cuts, -0.22, 0.18)
    return jnp.clip(result, -limit, limit).astype(dtype)


def setup_inputs(seed: int = 0) -> dict:
    splits = jax.random.split(jax.random.key(seed), 8)
    return {
        "tokens": gaussian(splits[0], (REPLICAS, TOK_R, D), 1.0, 6.0, ((0, 128),)),
        "cotangent": gaussian(splits[1], (REPLICAS, TOK_R, FF), 0.02, 0.119628906, ((0, 128), (2, 8))),
        "adapter_a": gaussian(splits[2], (REPLICAS, R, D), 1.0, 6.0, ((0, 128), (2, 8)), jnp.float32),
        "adapter_b": gaussian(splits[3], (REPLICAS, R, FF), 1.0, 6.0, ((0, 128), (2, 8)), jnp.float32),
        "moment_a": gaussian(splits[4], (REPLICAS, R, D), 0.5, 3.0, ((0, 128), (2, 8)), jnp.float32),
        "moment_b": gaussian(splits[5], (REPLICAS, R, FF), 0.5, 3.0, ((0, 128), (2, 8)), jnp.float32),
        "step_start": jax.random.randint(splits[6], (1,), 0, 64).astype(jnp.int32),
    }


def replica_grads(operands):
    rows, cot, adapter_a, adapter_b = operands
    scale = jnp.float32(D) ** -0.5
    a16 = adapter_a.astype(jnp.bfloat16)
    b16 = adapter_b.astype(jnp.bfloat16)
    low_u = (jnp.dot(rows, a16.T, preferred_element_type=jnp.float32) * scale).astype(jnp.bfloat16)
    low_v = jnp.dot(cot, b16.T, preferred_element_type=jnp.float32).astype(jnp.bfloat16)
    grad_b = jnp.dot(low_u.T, cot, preferred_element_type=jnp.float32)
    grad_a = jnp.dot(low_v.T, rows, preferred_element_type=jnp.float32) * scale
    return grad_a, grad_b


def make_roll(bit):
    def rolled(values):
        return (jnp.roll(values[0], 1 << bit, axis=0), jnp.roll(values[1], 1 << bit, axis=0))
    return rolled


def reference(tokens, cotangent, adapter_a, adapter_b, moment_a, moment_b, step_start):
    levels = N_REP.bit_length() - 1
    for step in range(STEPS):
        level = ((step_start[0] + step) % levels).astype(jnp.int32)
        grad_a, grad_b = lax.map(replica_grads, (tokens, cotangent, adapter_a, adapter_b))
        moment_a = 0.9 * moment_a + grad_a
        moment_b = 0.9 * moment_b + grad_b
        next_a = adapter_a - 0.3 * moment_a
        next_b = adapter_b - 0.3 * moment_b
        recv_a, recv_b = lax.switch(level, [make_roll(bit) for bit in range(levels)], (next_a, next_b))
        adapter_a = 0.5 * (next_a + recv_a)
        adapter_b = 0.5 * (next_b + recv_b)
    return adapter_a, adapter_b
```

```python
import jax
import jax.numpy as jnp
from jax import lax
from jax.sharding import PartitionSpec as P

STEPS = 3


learn_rate = 0.3
beta_moment = 0.9


def shifted(block, axis, distance):
    devices = range(lax.axis_size(axis))
    route = [((i - distance) % len(devices), i) for i in devices]
    return lax.ppermute(block, axis, route)


def partner_after(values, level, levels):

    def make(bit):

        def moved(field):
            return shifted(field, "rep", 1 << bit)

        return moved

    return lax.switch(level, [make(bit) for bit in range(levels)], values)


def fsdp_sum(part):
    total = part
    for distance in range(1, lax.axis_size("fsdp")):
        total = total + shifted(part, "fsdp", distance)
    return total


def contract_rows(left, right):
    return lax.dot_general(
        left, right, (((1,), (1,)), ((), ())), preferred_element_type=jnp.float32
    )


def contract_tokens(left, right):
    return lax.dot_general(
        left, right, (((0,), (0,)), ((), ())), preferred_element_type=jnp.float32
    )


def shards(tokens, cotangent, adapter_a, adapter_b, moment_a, moment_b, step_start):
    rows = tokens[0]
    cot = cotangent[0]
    factor_a = adapter_a[0]
    factor_b = adapter_b[0]
    moment_da = moment_a[0]
    moment_db = moment_b[0]
    scale = jnp.float32(rows.shape[1]) ** (-0.5)
    own_width = factor_a.shape[1]
    rank = factor_a.shape[0]
    offset = lax.axis_index("fsdp") * own_width
    own_cols = lax.dynamic_slice_in_dim(rows, offset, own_width, 1)
    levels = lax.axis_size("rep").bit_length() - 1
    for step in range(STEPS):
        level = (step_start[0] + step) % levels
        a16 = factor_a.astype(jnp.bfloat16)
        b16 = factor_b.astype(jnp.bfloat16)
        part_u = contract_rows(own_cols, a16)
        part_v = contract_rows(cot, b16)
        total = fsdp_sum(jnp.concatenate([part_u, part_v], axis=1))
        low_u = (total[:, :rank] * scale).astype(jnp.bfloat16)
        low_v = total[:, rank:].astype(jnp.bfloat16)
        grad_b = contract_tokens(low_u, cot)
        grad_a = contract_tokens(low_v, own_cols) * scale
        moment_da = beta_moment * moment_da + grad_a
        moment_db = beta_moment * moment_db + grad_b
        stepped = jnp.concatenate(
            [factor_a - learn_rate * moment_da, factor_b - learn_rate * moment_db], axis=1
        )
        merged = 0.5 * (stepped + partner_after(stepped, level, levels))
        factor_a = merged[:, :own_width]
        factor_b = merged[:, own_width:]
    return (factor_a[None], factor_b[None])


def solution(mesh):
    in_specs = (
        P("rep", None, None),
        P("rep", None, "fsdp"),
        P("rep", None, "fsdp"),
        P("rep", None, "fsdp"),
        P("rep", None, "fsdp"),
        P("rep", None, "fsdp"),
        P(),
    )
    out_specs = (P("rep", None, "fsdp"), P("rep", None, "fsdp"))
    return jax.shard_map(shards, mesh=mesh, in_specs=in_specs, out_specs=out_specs, check_vma=False)
```

```python
import jax
import jax.numpy as jnp
from jax import lax
from jax.sharding import PartitionSpec as P

STEPS = 3


learn_rate = 0.3
beta_moment = 0.9


def shifted(block, axis, distance):
    devices = range(lax.axis_size(axis))
    route = [((i - distance) % len(devices), i) for i in devices]
    return lax.ppermute(block, axis, route)


def partner_after(values, level, levels):

    def make(bit):

        def moved(field):
            return shifted(field, "rep", 1 << bit)

        return moved

    return lax.switch(level, [make(bit) for bit in range(levels)], values)


def fsdp_sum(total):
    size = lax.axis_size("fsdp")
    bit = 1
    while bit < size:
        route = [(i, i ^ bit) for i in range(size)]
        total = total + lax.ppermute(total, "fsdp", route)
        bit *= 2
    return total


def contract_rows(left, right):
    return lax.dot_general(
        left, right, (((1,), (1,)), ((), ())), preferred_element_type=jnp.float32
    )


def contract_tokens(left, right):
    return lax.dot_general(
        left, right, (((0,), (0,)), ((), ())), preferred_element_type=jnp.float32
    )


def shards(tokens, cotangent, adapter_a, adapter_b, moment_a, moment_b, step_start):
    rows = tokens[0]
    cot = cotangent[0]
    factor_a = adapter_a[0]
    factor_b = adapter_b[0]
    moment_da = moment_a[0]
    moment_db = moment_b[0]
    scale = jnp.float32(rows.shape[1]) ** (-0.5)
    own_width = factor_a.shape[1]
    rank = factor_a.shape[0]
    offset = lax.axis_index("fsdp") * own_width
    own_cols = lax.dynamic_slice_in_dim(rows, offset, own_width, 1)
    levels = lax.axis_size("rep").bit_length() - 1
    for step in range(STEPS):
        level = (step_start[0] + step) % levels
        a16 = factor_a.astype(jnp.bfloat16)
        b16 = factor_b.astype(jnp.bfloat16)
        part_u = contract_rows(own_cols, a16)
        part_v = contract_rows(cot, b16)
        total = fsdp_sum(jnp.concatenate([part_u, part_v], axis=1))
        low_u = (total[:, :rank] * scale).astype(jnp.bfloat16)
        low_v = total[:, rank:].astype(jnp.bfloat16)
        grad_b = contract_tokens(low_u, cot)
        grad_a = contract_tokens(low_v, own_cols) * scale
        moment_da = beta_moment * moment_da + grad_a
        moment_db = beta_moment * moment_db + grad_b
        stepped = jnp.concatenate(
            [factor_a - learn_rate * moment_da, factor_b - learn_rate * moment_db], axis=1
        )
        merged = 0.5 * (stepped + partner_after(stepped, level, levels))
        factor_a = merged[:, :own_width]
        factor_b = merged[:, own_width:]
    return (factor_a[None], factor_b[None])


def solution(mesh):
    in_specs = (
        P("rep", None, None),
        P("rep", None, "fsdp"),
        P("rep", None, "fsdp"),
        P("rep", None, "fsdp"),
        P("rep", None, "fsdp"),
        P("rep", None, "fsdp"),
        P(),
    )
    out_specs = (P("rep", None, "fsdp"), P("rep", None, "fsdp"))
    return jax.shard_map(shards, mesh=mesh, in_specs=in_specs, out_specs=out_specs, check_vma=False)
```

```python
import jax
import jax.numpy as jnp
from jax import lax
from jax.sharding import PartitionSpec as P

STEPS = 3


learn_rate = 0.3
beta_moment = 0.9


def shifted(block, axis, distance):
    devices = range(lax.axis_size(axis))
    route = [((i - distance) % len(devices), i) for i in devices]
    return lax.ppermute(block, axis, route)


def partner_after(values, level, levels):

    def make(bit):

        def moved(field):
            return shifted(field, "rep", 1 << bit)

        return moved

    return lax.switch(level, [make(bit) for bit in range(levels)], values)


def fsdp_sum(total):
    size = lax.axis_size("fsdp")
    bit = 1
    while bit < size:
        route = [(i, i ^ bit) for i in range(size)]
        sent = lax.ppermute(total.astype(jnp.bfloat16), "fsdp", route)
        total = total + sent.astype(jnp.float32)
        bit *= 2
    return total


def contract_rows(left, right):
    return lax.dot_general(
        left, right, (((1,), (1,)), ((), ())), preferred_element_type=jnp.float32
    )


def contract_tokens(left, right):
    return lax.dot_general(
        left, right, (((0,), (0,)), ((), ())), preferred_element_type=jnp.float32
    )


def shards(tokens, cotangent, adapter_a, adapter_b, moment_a, moment_b, step_start):
    rows = tokens[0]
    cot = cotangent[0]
    factor_a = adapter_a[0]
    factor_b = adapter_b[0]
    moment_da = moment_a[0]
    moment_db = moment_b[0]
    scale = jnp.float32(rows.shape[1]) ** (-0.5)
    own_width = factor_a.shape[1]
    rank = factor_a.shape[0]
    offset = lax.axis_index("fsdp") * own_width
    own_cols = lax.dynamic_slice_in_dim(rows, offset, own_width, 1)
    levels = lax.axis_size("rep").bit_length() - 1
    for step in range(STEPS):
        level = (step_start[0] + step) % levels
        a16 = factor_a.astype(jnp.bfloat16)
        b16 = factor_b.astype(jnp.bfloat16)
        part_u = contract_rows(own_cols, a16)
        part_v = contract_rows(cot, b16)
        total = fsdp_sum(jnp.concatenate([part_u, part_v], axis=1))
        low_u = (total[:, :rank] * scale).astype(jnp.bfloat16)
        low_v = total[:, rank:].astype(jnp.bfloat16)
        grad_b = contract_tokens(low_u, cot)
        grad_a = contract_tokens(low_v, own_cols) * scale
        moment_da = beta_moment * moment_da + grad_a
        moment_db = beta_moment * moment_db + grad_b
        stepped = jnp.concatenate(
            [factor_a - learn_rate * moment_da, factor_b - learn_rate * moment_db], axis=1
        )
        received = partner_after(stepped.astype(jnp.bfloat16), level, levels)
        merged = 0.5 * (stepped + received.astype(jnp.float32))
        factor_a = merged[:, :own_width]
        factor_b = merged[:, own_width:]
    return (factor_a[None], factor_b[None])


def solution(mesh):
    in_specs = (
        P("rep", None, None),
        P("rep", None, "fsdp"),
        P("rep", None, "fsdp"),
        P("rep", None, "fsdp"),
        P("rep", None, "fsdp"),
        P("rep", None, "fsdp"),
        P(),
    )
    out_specs = (P("rep", None, "fsdp"), P("rep", None, "fsdp"))
    return jax.shard_map(shards, mesh=mesh, in_specs=in_specs, out_specs=out_specs, check_vma=False)
```

```python
import jax
import jax.numpy as jnp
from jax import lax
from jax.sharding import PartitionSpec as P

STEPS = 3
CHUNKS = 2


learn_rate = 0.3
beta_moment = 0.9


def shifted(block, axis, distance):
    devices = range(lax.axis_size(axis))
    route = [((i - distance) % len(devices), i) for i in devices]
    return lax.ppermute(block, axis, route)


def partner_after(values, level, levels):

    def make(bit):

        def moved(field):
            return shifted(field, "rep", 1 << bit)

        return moved

    return lax.switch(level, [make(bit) for bit in range(levels)], values)


def fsdp_sum(total):
    size = lax.axis_size("fsdp")
    bit = 1
    while bit < size:
        route = [(i, i ^ bit) for i in range(size)]
        sent = lax.ppermute(total.astype(jnp.bfloat16), "fsdp", route)
        total = total + sent.astype(jnp.float32)
        bit *= 2
    return total


def contract_rows(left, right):
    return lax.dot_general(
        left, right, (((1,), (1,)), ((), ())), preferred_element_type=jnp.float32
    )


def contract_tokens(left, right):
    return lax.dot_general(
        left, right, (((0,), (0,)), ((), ())), preferred_element_type=jnp.float32
    )


def chain(rows, cot, own_cols, factor_a, factor_b, moment_da, moment_db, first):
    scale = jnp.float32(rows.shape[1]) ** (-0.5)
    own_width = factor_a.shape[1]
    rank = factor_a.shape[0]
    levels = lax.axis_size("rep").bit_length() - 1
    for step in range(STEPS):
        level = (first + step) % levels
        a16 = factor_a.astype(jnp.bfloat16)
        b16 = factor_b.astype(jnp.bfloat16)
        part_u = contract_rows(own_cols, a16)
        part_v = contract_rows(cot, b16)
        total = fsdp_sum(jnp.concatenate([part_u, part_v], axis=1))
        low_u = (total[:, :rank] * scale).astype(jnp.bfloat16)
        low_v = total[:, rank:].astype(jnp.bfloat16)
        grad_b = contract_tokens(low_u, cot)
        grad_a = contract_tokens(low_v, own_cols) * scale
        moment_da = beta_moment * moment_da + grad_a
        moment_db = beta_moment * moment_db + grad_b
        stepped = jnp.concatenate(
            [factor_a - learn_rate * moment_da, factor_b - learn_rate * moment_db], axis=1
        )
        received = shifted(stepped.astype(jnp.bfloat16), "rep", 1 << level)
        merged = 0.5 * (stepped + received.astype(jnp.float32))
        factor_a = merged[:, :own_width]
        factor_b = merged[:, own_width:]
    return factor_a, factor_b


def shards(tokens, cotangent, adapter_a, adapter_b, moment_a, moment_b, step_start):
    rows = tokens[0]
    cot = cotangent[0]
    own_width = adapter_a.shape[2]
    offset = lax.axis_index("fsdp") * own_width
    own_cols = lax.dynamic_slice_in_dim(rows, offset, own_width, 1)
    rank = adapter_a.shape[1]
    piece = rank // CHUNKS
    levels = lax.axis_size("rep").bit_length() - 1

    def make(first):

        def run(operands):
            rows, cot, own_cols, adapter_a, adapter_b, moment_a, moment_b = operands
            outs_a, outs_b = [], []
            for chunk in range(CHUNKS):
                lo = chunk * piece
                pick = lambda x: x[0, lo : lo + piece]
                fa, fb = chain(
                    rows, cot, own_cols, pick(adapter_a), pick(adapter_b), pick(moment_a), pick(moment_b), first
                )
                outs_a.append(fa)
                outs_b.append(fb)
            return (jnp.concatenate(outs_a, 0)[None], jnp.concatenate(outs_b, 0)[None])

        return run

    operands = (rows, cot, own_cols, adapter_a, adapter_b, moment_a, moment_b)
    return lax.switch(step_start[0] % levels, [make(first) for first in range(levels)], operands)


def solution(mesh):
    in_specs = (
        P("rep", None, None),
        P("rep", None, "fsdp"),
        P("rep", None, "fsdp"),
        P("rep", None, "fsdp"),
        P("rep", None, "fsdp"),
        P("rep", None, "fsdp"),
        P(),
    )
    out_specs = (P("rep", None, "fsdp"), P("rep", None, "fsdp"))
    return jax.shard_map(shards, mesh=mesh, in_specs=in_specs, out_specs=out_specs, check_vma=False)
```

```python
import jax
import jax.numpy as jnp
from jax import lax
from jax.sharding import PartitionSpec as P

STEPS = 3


learn_rate = 0.3
beta_moment = 0.9


def shifted(block, axis, distance):
    devices = range(lax.axis_size(axis))
    route = [((i - distance) % len(devices), i) for i in devices]
    return lax.ppermute(block, axis, route)


def partner_after(values, level, levels):

    def make(bit):

        def moved(field):
            return shifted(field, "rep", 1 << bit)

        return moved

    return lax.switch(level, [make(bit) for bit in range(levels)], values)


def fsdp_sum(part):
    size = lax.axis_size("fsdp")
    spread = jnp.broadcast_to(part.astype(jnp.bfloat16)[None], (size,) + part.shape)
    gathered = lax.all_to_all(spread, "fsdp", 0, 0)
    return jnp.sum(gathered.astype(jnp.float32), axis=0)


def contract_rows(left, right):
    return lax.dot_general(
        left, right, (((1,), (1,)), ((), ())), preferred_element_type=jnp.float32
    )


def contract_tokens(left, right):
    return lax.dot_general(
        left, right, (((0,), (0,)), ((), ())), preferred_element_type=jnp.float32
    )


def shards(tokens, cotangent, adapter_a, adapter_b, moment_a, moment_b, step_start):
    rows = tokens[0]
    cot = cotangent[0]
    factor_a = adapter_a[0]
    factor_b = adapter_b[0]
    moment_da = moment_a[0]
    moment_db = moment_b[0]
    scale = jnp.float32(rows.shape[1]) ** (-0.5)
    own_width = factor_a.shape[1]
    rank = factor_a.shape[0]
    offset = lax.axis_index("fsdp") * own_width
    own_cols = lax.dynamic_slice_in_dim(rows, offset, own_width, 1)
    levels = lax.axis_size("rep").bit_length() - 1
    for step in range(STEPS):
        level = (step_start[0] + step) % levels
        a16 = factor_a.astype(jnp.bfloat16)
        b16 = factor_b.astype(jnp.bfloat16)
        part_u = contract_rows(own_cols, a16)
        part_v = contract_rows(cot, b16)
        total = fsdp_sum(jnp.concatenate([part_u, part_v], axis=1))
        low_u = (total[:, :rank] * scale).astype(jnp.bfloat16)
        low_v = total[:, rank:].astype(jnp.bfloat16)
        grad_b = contract_tokens(low_u, cot)
        grad_a = contract_tokens(low_v, own_cols) * scale
        moment_da = beta_moment * moment_da + grad_a
        moment_db = beta_moment * moment_db + grad_b
        stepped = jnp.concatenate(
            [factor_a - learn_rate * moment_da, factor_b - learn_rate * moment_db], axis=1
        )
        received = partner_after(stepped.astype(jnp.bfloat16), level, levels)
        merged = 0.5 * (stepped + received.astype(jnp.float32))
        factor_a = merged[:, :own_width]
        factor_b = merged[:, own_width:]
    return (factor_a[None], factor_b[None])


def solution(mesh):
    in_specs = (
        P("rep", None, None),
        P("rep", None, "fsdp"),
        P("rep", None, "fsdp"),
        P("rep", None, "fsdp"),
        P("rep", None, "fsdp"),
        P("rep", None, "fsdp"),
        P(),
    )
    out_specs = (P("rep", None, "fsdp"), P("rep", None, "fsdp"))
    return jax.shard_map(shards, mesh=mesh, in_specs=in_specs, out_specs=out_specs, check_vma=False)
```

```python
import jax
import jax.numpy as jnp
from jax import lax
from jax.sharding import PartitionSpec as P

STEPS = 3


learn_rate = 0.3
beta_moment = 0.9


def shifted(block, axis, distance):
    devices = range(lax.axis_size(axis))
    route = [((i - distance) % len(devices), i) for i in devices]
    return lax.ppermute(block, axis, route)


def partner_after(values, level, levels):

    def make(bit):

        def moved(field):
            size = lax.axis_size("rep")
            if 2 << bit != size or size < 4:
                return shifted(field, "rep", 1 << bit)
            half = field.shape[0] // 2
            ahead = shifted(field[:half], "rep", 1 << bit)
            back = shifted(shifted(field[half:], "rep", -(size // 4)), "rep", -(size // 4))
            return jnp.concatenate([ahead, back], axis=0)

        return moved

    return lax.switch(level, [make(bit) for bit in range(levels)], values)


def fsdp_sum(part):
    size = lax.axis_size("fsdp")
    spread = jnp.broadcast_to(part.astype(jnp.bfloat16)[None], (size,) + part.shape)
    gathered = lax.all_to_all(spread, "fsdp", 0, 0)
    return jnp.sum(gathered.astype(jnp.float32), axis=0)


def contract_rows(left, right):
    return lax.dot_general(
        left, right, (((1,), (1,)), ((), ())), preferred_element_type=jnp.float32
    )


def contract_tokens(left, right):
    return lax.dot_general(
        left, right, (((0,), (0,)), ((), ())), preferred_element_type=jnp.float32
    )


def shards(tokens, cotangent, adapter_a, adapter_b, moment_a, moment_b, step_start):
    rows = tokens[0]
    cot = cotangent[0]
    factor_a = adapter_a[0]
    factor_b = adapter_b[0]
    moment_da = moment_a[0]
    moment_db = moment_b[0]
    scale = jnp.float32(rows.shape[1]) ** (-0.5)
    own_width = factor_a.shape[1]
    rank = factor_a.shape[0]
    offset = lax.axis_index("fsdp") * own_width
    own_cols = lax.dynamic_slice_in_dim(rows, offset, own_width, 1)
    levels = lax.axis_size("rep").bit_length() - 1
    for step in range(STEPS):
        level = (step_start[0] + step) % levels
        a16 = factor_a.astype(jnp.bfloat16)
        b16 = factor_b.astype(jnp.bfloat16)
        part_u = contract_rows(own_cols, a16)
        part_v = contract_rows(cot, b16)
        total = fsdp_sum(jnp.concatenate([part_u, part_v], axis=1))
        low_u = (total[:, :rank] * scale).astype(jnp.bfloat16)
        low_v = total[:, rank:].astype(jnp.bfloat16)
        grad_b = contract_tokens(low_u, cot)
        grad_a = contract_tokens(low_v, own_cols) * scale
        moment_da = beta_moment * moment_da + grad_a
        moment_db = beta_moment * moment_db + grad_b
        stepped = jnp.concatenate(
            [factor_a - learn_rate * moment_da, factor_b - learn_rate * moment_db], axis=1
        )
        received = partner_after(stepped.astype(jnp.bfloat16), level, levels)
        merged = 0.5 * (stepped + received.astype(jnp.float32))
        factor_a = merged[:, :own_width]
        factor_b = merged[:, own_width:]
    return (factor_a[None], factor_b[None])


def solution(mesh):
    in_specs = (
        P("rep", None, None),
        P("rep", None, "fsdp"),
        P("rep", None, "fsdp"),
        P("rep", None, "fsdp"),
        P("rep", None, "fsdp"),
        P("rep", None, "fsdp"),
        P(),
    )
    out_specs = (P("rep", None, "fsdp"), P("rep", None, "fsdp"))
    return jax.shard_map(shards, mesh=mesh, in_specs=in_specs, out_specs=out_specs, check_vma=False)
```

```python
import jax
import jax.numpy as jnp
from jax import lax
from jax.sharding import PartitionSpec as P

STEPS = 3


learn_rate = 0.3
beta_moment = 0.9


def shifted(block, axis, distance):
    devices = range(lax.axis_size(axis))
    route = [((i - distance) % len(devices), i) for i in devices]
    return lax.ppermute(block, axis, route)


def partner_after(values, level, levels):

    def make(bit):

        def moved(field):
            return shifted(field, "rep", 1 << bit)

        return moved

    return lax.switch(level, [make(bit) for bit in range(levels)], values)


def fsdp_sum(part):
    size = lax.axis_size("fsdp")
    spread = jnp.broadcast_to(part.astype(jnp.bfloat16)[None], (size,) + part.shape)
    gathered = lax.all_to_all(spread, "fsdp", 0, 0)
    return jnp.sum(gathered.astype(jnp.float32), axis=0)


def contract_rows(left, right):
    return lax.dot_general(
        left, right, (((1,), (1,)), ((), ())), preferred_element_type=jnp.float32
    )


def contract_tokens(left, right):
    return lax.dot_general(
        left, right, (((0,), (0,)), ((), ())), preferred_element_type=jnp.float32
    )


def shards(tokens, cotangent, adapter_a, adapter_b, moment_a, moment_b, step_start):
    rows = tokens[0]
    cot = cotangent[0]
    factor_a = adapter_a[0]
    factor_b = adapter_b[0]
    moment_da = moment_a[0]
    moment_db = moment_b[0]
    scale = jnp.float32(rows.shape[1]) ** (-0.5)
    own_width = factor_a.shape[1]
    rank = factor_a.shape[0]
    offset = lax.axis_index("fsdp") * own_width
    own_cols = lax.dynamic_slice_in_dim(rows, offset, own_width, 1)
    levels = lax.axis_size("rep").bit_length() - 1
    both = jnp.concatenate([own_cols, cot], axis=1)
    for step in range(STEPS):
        level = (step_start[0] + step) % levels
        a16 = factor_a.astype(jnp.bfloat16)
        b16 = factor_b.astype(jnp.bfloat16)
        weights = jnp.concatenate(
            [
                jnp.concatenate([a16, jnp.zeros((rank, b16.shape[1]), jnp.bfloat16)], axis=1),
                jnp.concatenate([jnp.zeros((rank, own_width), jnp.bfloat16), b16], axis=1),
            ],
            axis=0,
        )
        total = fsdp_sum(contract_rows(both, weights))
        low = jnp.concatenate(
            [(total[:, :rank] * scale).astype(jnp.bfloat16), total[:, rank:].astype(jnp.bfloat16)], axis=1
        )
        grads = contract_tokens(low, both)
        grad_b = grads[:rank, own_width:]
        grad_a = grads[rank:, :own_width] * scale
        moment_da = beta_moment * moment_da + grad_a
        moment_db = beta_moment * moment_db + grad_b
        stepped = jnp.concatenate(
            [factor_a - learn_rate * moment_da, factor_b - learn_rate * moment_db], axis=1
        )
        received = partner_after(stepped.astype(jnp.bfloat16), level, levels)
        merged = 0.5 * (stepped + received.astype(jnp.float32))
        factor_a = merged[:, :own_width]
        factor_b = merged[:, own_width:]
    return (factor_a[None], factor_b[None])


def solution(mesh):
    in_specs = (
        P("rep", None, None),
        P("rep", None, "fsdp"),
        P("rep", None, "fsdp"),
        P("rep", None, "fsdp"),
        P("rep", None, "fsdp"),
        P("rep", None, "fsdp"),
        P(),
    )
    out_specs = (P("rep", None, "fsdp"), P("rep", None, "fsdp"))
    return jax.shard_map(shards, mesh=mesh, in_specs=in_specs, out_specs=out_specs, check_vma=False)
```

```python
import jax
import jax.numpy as jnp
from jax import lax
from jax.sharding import PartitionSpec as P

STEPS = 3


learn_rate = 0.3
beta_moment = 0.9


def shifted(block, axis, distance):
    devices = range(lax.axis_size(axis))
    route = [((i - distance) % len(devices), i) for i in devices]
    return lax.ppermute(block, axis, route)


def partner_after(values, level, levels):

    def make(bit):

        def moved(field):
            return shifted(field, "rep", 1 << bit)

        return moved

    return lax.switch(level, [make(bit) for bit in range(levels)], values)


def fsdp_sum(part):
    size = lax.axis_size("fsdp")
    spread = jnp.broadcast_to(part.astype(jnp.bfloat16)[None], (size,) + part.shape)
    gathered = lax.all_to_all(spread, "fsdp", 0, 0)
    return jnp.sum(gathered.astype(jnp.float32), axis=0)


def contract_rows(left, right):
    return lax.dot_general(
        left, right, (((1,), (1,)), ((), ())), preferred_element_type=jnp.float32
    )


def contract_tokens(left, right):
    return lax.dot_general(
        left, right, (((0,), (0,)), ((), ())), preferred_element_type=jnp.float32
    )


def shards(tokens, cotangent, adapter_a, adapter_b, moment_a, moment_b, step_start):
    rows = tokens[0]
    cot = cotangent[0]
    factor_a = adapter_a[0]
    factor_b = adapter_b[0]
    moment_da = moment_a[0]
    moment_db = moment_b[0]
    scale = jnp.float32(rows.shape[1]) ** (-0.5)
    own_width = factor_a.shape[1]
    rank = factor_a.shape[0]
    offset = lax.axis_index("fsdp") * own_width
    own_cols = lax.dynamic_slice_in_dim(rows, offset, own_width, 1)
    levels = lax.axis_size("rep").bit_length() - 1
    for step in range(STEPS):
        level = (step_start[0] + step) % levels
        a16 = factor_a.astype(jnp.bfloat16)
        b16 = factor_b.astype(jnp.bfloat16)
        part_u = contract_rows(own_cols, a16)
        part_v = contract_rows(cot, b16)
        total = fsdp_sum(jnp.concatenate([part_u, part_v], axis=1))
        low_u = (total[:, :rank] * scale).astype(jnp.bfloat16)
        low_v = total[:, rank:].astype(jnp.bfloat16)
        grad_b = contract_tokens(low_u, cot)
        grad_a = contract_tokens(low_v, own_cols) * scale
        moment_da = beta_moment * moment_da + grad_a
        moment_db = beta_moment * moment_db + grad_b
        stepped = jnp.concatenate(
            [factor_a - learn_rate * moment_da, factor_b - learn_rate * moment_db], axis=1
        )
        received = partner_after(stepped.astype(jnp.bfloat16), level, levels)
        factor_a = 0.5 * (stepped[:, :own_width] + received[:, :own_width].astype(jnp.float32))
        factor_b = 0.5 * (stepped[:, own_width:] + received[:, own_width:].astype(jnp.float32))
    return (factor_a[None], factor_b[None])


def solution(mesh):
    in_specs = (
        P("rep", None, None),
        P("rep", None, "fsdp"),
        P("rep", None, "fsdp"),
        P("rep", None, "fsdp"),
        P("rep", None, "fsdp"),
        P("rep", None, "fsdp"),
        P(),
    )
    out_specs = (P("rep", None, "fsdp"), P("rep", None, "fsdp"))
    return jax.shard_map(shards, mesh=mesh, in_specs=in_specs, out_specs=out_specs, check_vma=False)
```

```python
import jax
import jax.numpy as jnp
from jax import lax
from jax.sharding import PartitionSpec as P

STEPS = 3


learn_rate = 0.3
beta_moment = 0.9


def shifted(block, axis, distance):
    devices = range(lax.axis_size(axis))
    route = [((i - distance) % len(devices), i) for i in devices]
    return lax.ppermute(block, axis, route)


def partner_after(values, level, levels):

    def make(bit):

        def moved(field):
            return shifted(field, "rep", 1 << bit)

        return moved

    return lax.switch(level, [make(bit) for bit in range(levels)], values)


def fsdp_lows(part, rank, scale):
    size = lax.axis_size("fsdp")
    tokens, width = part.shape
    pieces = part.astype(jnp.bfloat16).reshape(size, tokens // size, width)
    mine = jnp.sum(lax.all_to_all(pieces, "fsdp", 0, 0).astype(jnp.float32), axis=0)
    low = jnp.concatenate(
        [(mine[:, :rank] * scale).astype(jnp.bfloat16), mine[:, rank:].astype(jnp.bfloat16)], axis=1
    )
    spread = jnp.broadcast_to(low[None], (size,) + low.shape)
    return lax.all_to_all(spread, "fsdp", 0, 0).reshape(tokens, width)


def contract_rows(left, right):
    return lax.dot_general(
        left, right, (((1,), (1,)), ((), ())), preferred_element_type=jnp.float32
    )


def contract_tokens(left, right):
    return lax.dot_general(
        left, right, (((0,), (0,)), ((), ())), preferred_element_type=jnp.float32
    )


def shards(tokens, cotangent, adapter_a, adapter_b, moment_a, moment_b, step_start):
    rows = tokens[0]
    cot = cotangent[0]
    factor_a = adapter_a[0]
    factor_b = adapter_b[0]
    moment_da = moment_a[0]
    moment_db = moment_b[0]
    scale = jnp.float32(rows.shape[1]) ** (-0.5)
    own_width = factor_a.shape[1]
    rank = factor_a.shape[0]
    offset = lax.axis_index("fsdp") * own_width
    own_cols = lax.dynamic_slice_in_dim(rows, offset, own_width, 1)
    levels = lax.axis_size("rep").bit_length() - 1
    for step in range(STEPS):
        level = (step_start[0] + step) % levels
        a16 = factor_a.astype(jnp.bfloat16)
        b16 = factor_b.astype(jnp.bfloat16)
        part_u = contract_rows(own_cols, a16)
        part_v = contract_rows(cot, b16)
        low = fsdp_lows(jnp.concatenate([part_u, part_v], axis=1), rank, scale)
        low_u = low[:, :rank]
        low_v = low[:, rank:]
        grad_b = contract_tokens(low_u, cot)
        grad_a = contract_tokens(low_v, own_cols) * scale
        moment_da = beta_moment * moment_da + grad_a
        moment_db = beta_moment * moment_db + grad_b
        stepped = jnp.concatenate(
            [factor_a - learn_rate * moment_da, factor_b - learn_rate * moment_db], axis=1
        )
        received = partner_after(stepped.astype(jnp.bfloat16), level, levels)
        merged = 0.5 * (stepped + received.astype(jnp.float32))
        factor_a = merged[:, :own_width]
        factor_b = merged[:, own_width:]
    return (factor_a[None], factor_b[None])


def solution(mesh):
    in_specs = (
        P("rep", None, None),
        P("rep", None, "fsdp"),
        P("rep", None, "fsdp"),
        P("rep", None, "fsdp"),
        P("rep", None, "fsdp"),
        P("rep", None, "fsdp"),
        P(),
    )
    out_specs = (P("rep", None, "fsdp"), P("rep", None, "fsdp"))
    return jax.shard_map(shards, mesh=mesh, in_specs=in_specs, out_specs=out_specs, check_vma=False)
```
